256 devices in a mesh: hyp: 32 (over y, x, core), head: 8 (over z).
Axes of the slice: x: 4, y: 4, z: 8, core: 2. Of those that a mesh axis runs over, the one named last changes fastest.
Arguments:
- step_embeds: bfloat16 [3, 512, 4096], P(None, 'hyp'), may hold values from -6 to 6
- lang_table: bfloat16 [8, 4096], replicated, may hold values from -3 to 3
- lang_ids: int32 [32, 4], replicated, may hold values from 0 to 7
- self_gain: float32 [4096], replicated, may hold values from 0.1 to 1.9
- self_wq: bfloat16 [4096, 2048], P(None, 'head'), may hold values from -0.09375 to 0.09375
- self_wk: bfloat16 [4096, 2048], P(None, 'head'), may hold values from -0.09375 to 0.09375
- self_wv: bfloat16 [4096, 2048], P(None, 'head'), may hold values from -0.09375 to 0.09375
- self_wo: bfloat16 [2048, 4096], P('head'), may hold values from -0.125 to 0.125
- cross_gain: float32 [4096], replicated, may hold values from 0.1 to 1.9
- cross_wq: bfloat16 [4096, 2048], P(None, 'head'), may hold values from -0.09375 to 0.09375
- cross_wkv: bfloat16 [4096, 4096], P('hyp', 'head'), may hold values from -0.09375 to 0.09375
- encoder_rows: bfloat16 [24576, 4096], P('hyp', 'head'), may hold values from -200 to 200
- doc_lengths: int32 [32], P('hyp'), may hold values from 192 to 768, as said below
- past_keys: bfloat16 [512, 32, 2048], P('hyp', None, 'head'), may hold values from -200 to 200
- past_values: bfloat16 [512, 32, 2048], P('hyp', None, 'head'), may hold values from -6 to 6
- parents: int32 [3, 512], replicated, may hold values from 0 to 3
Outputs:
- cross_context: bfloat16 [3, 512, 2048], P(None, 'hyp', 'head')
- final_keys: bfloat16 [512, 35, 2048], P('hyp', None, 'head')
- final_values: bfloat16 [512, 35, 2048], P('hyp', None, 'head')
The draws below stay inside these ranges and needn't reach their ends.
Inputs may be any that keep to these rules, and one draw needn't show every extreme that they name: `doc_lengths`: some document has exactly 768 live rows. `parents`: A parent is a beam of the same document and target.
All inputs are finite; a program needn't handle non-finite values.
Results may differ from the reference program's by a relative error of at most 0.03.
Values may be sent and summed in bfloat16 or wider, within the bound.
No kernel may reach another device: no remote copies, remote signals or barrier semaphores. Data moves between devices by JAX's collectives and lax.ppermute only.
A program may use at most 128 MiB of HBM per device.

```python
import jax
import jax.numpy as jnp
from jax import lax

D = 4096
HEADS = 8
HEAD = 256
BEAMS = 4
TARGETS = 4
LEN = 768
STEPS = 3
LANGS = 8
PAST = 32
DOCS = 32
HYPS = 512


def spiked_rows(key, row_total, col_total):
    base = jnp.clip(jax.random.normal(key, (row_total, col_total), jnp.float32), -4.0, 4.0)
    return base


def scaled_rows(key, row_total, col_total):
    base = jnp.clip(jax.random.normal(key, (row_total, col_total), jnp.float32), -4.0, 4.0)
    return base


def draw_encoder_rows(key, part):
    return scaled_rows(jax.random.fold_in(key, 3), DOCS * LEN, D).astype(jnp.bfloat16)


def draw_past_keys(key, part):
    flat = spiked_rows(jax.random.fold_in(key, 4), HYPS * PAST, HEADS * HEAD)
    return flat.reshape(HYPS, PAST, HEADS * HEAD).astype(jnp.bfloat16)


def draw_doc_lengths(key, part):
    lengths = jax.random.randint(jax.random.fold_in(key, 1), (DOCS,), LEN // 4, LEN + 1, jnp.int32)
    longest = jax.random.randint(jax.random.fold_in(key, 2), (), 0, DOCS, jnp.int32)
    return lengths.at[longest].set(LEN)


def place_ends(array, stream_key, low, largest):
    longest = array.shape.index(max(array.shape))
    spots = []
    for shift in (0, 1):
        where = [jax.random.randint(jax.random.fold_in(stream_key, axis), (), 0, length) for axis, length in enumerate(array.shape)]
        where[longest] = (where[longest] + shift) % array.shape[longest]
        spots.append(tuple(where))
    return array.at[spots[0]].set(low).at[spots[1]].set(largest)


def levels(own_key, shape, cuts, smallest, top_value):
    def one(position, parts):
        heights = jax.random.uniform(jax.random.fold_in(jax.random.fold_in(own_key, 6), position), (parts,), jnp.float32, smallest / len(cuts), top_value / len(cuts))
        return jnp.repeat(jnp.exp(heights), shape[position] // parts).reshape((-1,) + (1,) * (len(shape) - position - 1))

    level = one(*cuts[0])
    for cut in cuts[1:]:
        level = level * one(*cut)
    return level


def gaussian(own_key, shape, scale, reach, split=(), kind=jnp.bfloat16):
    values = jax.random.normal(own_key, shape, jnp.float32) * scale
    if len(split) > 0:
        values = levels(own_key, shape, split, -0.22, 0.18) * values
    return jnp.clip(values, min=-reach, max=reach).astype(kind)


def setup_inputs(seed: int = 0) -> dict:
    keys = jax.random.split(jax.random.key(seed), 17)
    return {
        "step_embeds": gaussian(keys[0], (STEPS, HYPS, D), 1.0, 6.0, ((1, 32),)),
        "lang_table": gaussian(keys[1], (LANGS, D), 0.5, 3.0),
        "lang_ids": place_ends(jax.random.randint(keys[2], (DOCS, TARGETS), 0, LANGS), jax.random.fold_in(keys[2], 1), 0, LANGS - 1).astype(jnp.int32),
        "self_gain": jnp.clip(1.0 + 0.18 * jax.random.normal(keys[3], (D,), jnp.float32), 0.1, 1.9),
        "self_wq": gaussian(keys[4], (D, HEADS * HEAD), D ** -0.5, 0.09375, ((1, 8),)),
        "self_wk": gaussian(keys[5], (D, HEADS * HEAD), D ** -0.5, 0.09375, ((1, 8),)),
        "self_wv": gaussian(keys[6], (D, HEADS * HEAD), D ** -0.5, 0.09375, ((1, 8),)),
        "self_wo": gaussian(keys[7], (HEADS * HEAD, D), (HEADS * HEAD) ** -0.5, 0.125, ((0, 8),)),
        "cross_gain": jnp.clip(1.0 + 0.18 * jax.random.normal(keys[8], (D,), jnp.float32), 0.1, 1.9),
        "cross_wq": gaussian(keys[9], (D, HEADS * HEAD), D ** -0.5, 0.09375, ((1, 8),)),
        "cross_wkv": gaussian(keys[10], (D, 2 * HEADS * HEAD), D ** -0.5, 0.09375, ((0, 32), (1, 8))),
        "encoder_rows": draw_encoder_rows(jax.random.fold_in(keys[16], 71), 0),
        "doc_lengths": draw_doc_lengths(jax.random.fold_in(keys[16], 71), 0),
        "past_keys": draw_past_keys(jax.random.fold_in(keys[16], 71), 0),
        "past_values": gaussian(keys[14], (HYPS, PAST, HEADS * HEAD), 1.0, 6.0, ((0, 32), (2, 8))),
        "parents": place_ends(jax.random.randint(keys[15], (STEPS, HYPS), 0, BEAMS), jax.random.fold_in(keys[15], 1), 0, BEAMS - 1).astype(jnp.int32),
    }


EPSILON = 1e-06

def rms_scaled(values_in, gain):
    mean_square = lax.optimization_barrier(jnp.mean(values_in * values_in, axis=-1, keepdims=True))
    return values_in * lax.rsqrt(mean_square + EPSILON) * gain

def cross_attend(inputs):
    queries, cross_keys, cross_values, doc_length = inputs
    scaling = HEAD ** (-0.5)
    scores = jnp.einsum('qhd,jhd->hqj', queries.astype(jnp.float32), cross_keys.astype(jnp.float32)) * scaling
    live_mask = jnp.arange(LEN, dtype=jnp.int32) < doc_length
    scores = jnp.where(live_mask[None, None, :], scores, -jnp.inf)
    highest = lax.optimization_barrier(jnp.max(scores, axis=2, keepdims=True))
    raw_weights = jnp.exp(scores - highest)
    totals = lax.optimization_barrier(jnp.sum(raw_weights, axis=2, keepdims=True))
    weights = (raw_weights / totals).astype(jnp.bfloat16)
    output = jnp.einsum('hqj,jhd->qhd', weights.astype(jnp.float32), cross_values.astype(jnp.float32))
    return output.astype(jnp.bfloat16)

def reference(step_embeds, lang_table, lang_ids, self_gain, self_wq, self_wk, self_wv, self_wo, cross_gain, cross_wq, cross_wkv, encoder_rows, doc_lengths, past_keys, past_values, parents):
    hyp_ids = jnp.arange(HYPS, dtype=jnp.int32)
    doc_of = hyp_ids // TARGETS % DOCS
    target_of = hyp_ids % TARGETS
    lang_rows = lang_table[lang_ids[doc_of, target_of]].astype(jnp.float32)

    def project(doc_rows):
        return jnp.dot(doc_rows, cross_wkv, preferred_element_type=jnp.float32).astype(jnp.bfloat16)
    cross_kv = lax.map(project, encoder_rows.reshape(DOCS, LEN, D)).reshape(DOCS, LEN, HEADS, 2, HEAD)
    cross_keys = cross_kv[:, :, :, 0, :]
    cross_values = cross_kv[:, :, :, 1, :]
    cache_keys, cache_values = (past_keys, past_values)
    scaling = HEAD ** (-0.5)
    contexts = []
    for step_idx in range(STEPS):
        source = (parents[step_idx] * DOCS + doc_of) * TARGETS + target_of
        cache_keys = cache_keys[source]
        cache_values = cache_values[source]
        hidden_in = step_embeds[step_idx].astype(jnp.float32) + lang_rows
        normed = rms_scaled(hidden_in, self_gain).astype(jnp.bfloat16)
        new_query = jnp.dot(normed, self_wq, preferred_element_type=jnp.float32).astype(jnp.bfloat16)
        new_key = jnp.dot(normed, self_wk, preferred_element_type=jnp.float32).astype(jnp.bfloat16)
        new_value = jnp.dot(normed, self_wv, preferred_element_type=jnp.float32).astype(jnp.bfloat16)
        cache_keys = jnp.concatenate([cache_keys, new_key[:, None, :]], axis=1)
        cache_values = jnp.concatenate([cache_values, new_value[:, None, :]], axis=1)
        query_f = new_query.astype(jnp.float32).reshape(HYPS, HEADS, HEAD)
        key_f = cache_keys.astype(jnp.float32).reshape(HYPS, -1, HEADS, HEAD)
        value_f = cache_values.astype(jnp.float32).reshape(HYPS, -1, HEADS, HEAD)
        scores = jnp.einsum('rhd,rphd->rhp', query_f, key_f) * scaling
        highest = lax.optimization_barrier(jnp.max(scores, axis=2, keepdims=True))
        raw_weights = jnp.exp(scores - highest)
        totals = lax.optimization_barrier(jnp.sum(raw_weights, axis=2))
        summed = jnp.einsum('rhp,rphd->rhd', raw_weights, value_f)
        self_context = (summed / totals[:, :, None]).reshape(HYPS, HEADS * HEAD).astype(jnp.bfloat16)
        residual = hidden_in + jnp.dot(self_context, self_wo, preferred_element_type=jnp.float32)
        normed_cross = rms_scaled(residual, cross_gain).astype(jnp.bfloat16)
        cross_query = jnp.dot(normed_cross, cross_wq, preferred_element_type=jnp.float32).astype(jnp.bfloat16)
        grouped = cross_query.reshape(BEAMS, DOCS, TARGETS, HEADS, HEAD).transpose(1, 0, 2, 3, 4).reshape(DOCS, BEAMS * TARGETS, HEADS, HEAD)
        attended = lax.map(cross_attend, (grouped, cross_keys, cross_values, doc_lengths))
        restored = attended.reshape(DOCS, BEAMS, TARGETS, HEADS * HEAD).transpose(1, 0, 2, 3).reshape(HYPS, HEADS * HEAD)
        contexts.append(restored)
    return (jnp.stack(contexts), cache_keys, cache_values)
```

```python
import jax
import jax.numpy as jnp
from jax import lax
from jax.sharding import PartitionSpec as P

HEAD = 256
BEAMS = 4
TARGETS = 4
STEPS = 3


EPSILON = 1e-06


def rms_scaled(values_in, gain):
    mean_square = jnp.mean(values_in * values_in, axis=-1, keepdims=True)
    return values_in * lax.rsqrt(mean_square + EPSILON) * gain


def pick_rows(candidates, selector, row_axis):
    shape_list = [1] * candidates[0].ndim
    shape_list[row_axis] = selector.shape[0]
    chosen = candidates[0]
    for position in range(1, len(candidates)):
        chosen = jnp.where((selector == position).reshape(shape_list), candidates[position], chosen)
    return chosen


def beam_copies(block, hyp_count, group_size):
    copies = [block]
    for hop in range(1, BEAMS):
        distance = hop * group_size
        route = [((i - distance) % hyp_count, i) for i in range(hyp_count)]
        copies.append(lax.ppermute(block, "hyp", route))
    return copies


def cross_attend(queries, cross_keys, cross_values, doc_length, scaling):
    scores = (
        jnp.einsum("qd,jd->qj", queries, cross_keys, preferred_element_type=jnp.float32) * scaling
    )
    live_mask = lax.broadcasted_iota(jnp.int32, (1, cross_keys.shape[0]), 1) < doc_length
    scores = jnp.where(live_mask, scores, -jnp.inf)
    highest = jnp.max(scores, axis=1, keepdims=True)
    raw_weights = jnp.exp(scores - highest)
    totals = jnp.sum(raw_weights, axis=1, keepdims=True)
    weights = (raw_weights / totals).astype(jnp.bfloat16)
    output = jnp.einsum("qj,jd->qd", weights, cross_values, preferred_element_type=jnp.float32)
    return output.astype(jnp.bfloat16)


def shards(
    step_embeds,
    lang_table,
    lang_ids,
    self_gain,
    self_wq,
    self_wk,
    self_wv,
    self_wo,
    cross_gain,
    cross_wq,
    cross_wkv,
    encoder_rows,
    doc_lengths,
    past_keys,
    past_values,
    parents,
):
    hyp_count = lax.axis_size("hyp")
    group_size = hyp_count // BEAMS
    my_index = lax.axis_index("hyp")
    my_beam = my_index // group_size
    my_slot = my_index % group_size
    steps = step_embeds.shape[0]
    row_count = step_embeds.shape[1]
    docs_here = row_count // TARGETS
    head_width = self_wq.shape[1]
    doc_count = lang_ids.shape[0]
    past_len = past_keys.shape[1]
    scaling = HEAD ** (-0.5)

    full_weights = lax.all_gather(cross_wkv, "hyp", axis=0, tiled=True)
    full_rows = lax.all_gather(encoder_rows, "head", axis=1, tiled=True)
    cross_kv = jnp.dot(full_rows, full_weights, preferred_element_type=jnp.float32).astype(
        jnp.bfloat16
    )
    cross_kv = cross_kv.reshape(encoder_rows.shape[0], 2, HEAD)
    cross_keys = cross_kv[:, 0, :]
    cross_values = cross_kv[:, 1, :]
    doc_length = doc_lengths[0]

    past_stack = jnp.stack([past_keys, past_values])
    past_all = beam_copies(past_stack, hyp_count, group_size)

    my_langs = lax.dynamic_slice_in_dim(lang_ids, my_slot * docs_here, docs_here, 0).reshape(row_count)
    one_hot = (
        my_langs[:, None] == lax.broadcasted_iota(jnp.int32, (1, lang_table.shape[0]), 1)
    ).astype(jnp.bfloat16)
    lang_rows = jnp.dot(one_hot, lang_table, preferred_element_type=jnp.float32)

    hidden_in = step_embeds.astype(jnp.float32) + lang_rows[None]
    normed = rms_scaled(hidden_in, self_gain).astype(jnp.bfloat16).reshape(steps * row_count, -1)
    new_query = jnp.dot(normed, self_wq, preferred_element_type=jnp.float32).astype(jnp.bfloat16)
    new_key = jnp.dot(normed, self_wk, preferred_element_type=jnp.float32).astype(jnp.bfloat16)
    new_value = jnp.dot(normed, self_wv, preferred_element_type=jnp.float32).astype(jnp.bfloat16)
    new_query = new_query.reshape(steps, row_count, head_width)
    fresh = jnp.stack([new_key, new_value]).reshape(2, steps, row_count, head_width)
    fresh_all = beam_copies(fresh, hyp_count, group_size)

    parent_view = parents.reshape(steps, BEAMS, doc_count * TARGETS)
    parent_of = lax.dynamic_slice_in_dim(parent_view, my_slot * row_count, row_count, 2)
    own_beam = jnp.full((row_count,), my_beam, jnp.int32)

    def hop_of(beam):
        return (my_beam - beam) % BEAMS

    def climb(step_idx, beam):
        return jnp.take_along_axis(parent_of[step_idx], beam[None, :], axis=0)[0]

    def cache_at(step_idx):
        ancestor = own_beam
        new_parts = [None] * (step_idx + 1)
        new_parts[step_idx] = fresh[:, step_idx]
        for back in range(step_idx, 0, -1):
            ancestor = climb(back, ancestor)
            new_parts[back - 1] = pick_rows(
                [f[:, back - 1] for f in fresh_all], hop_of(ancestor), 1
            )
        ancestor = climb(0, ancestor)
        past_part = pick_rows(past_all, hop_of(ancestor), 1)
        return jnp.concatenate([past_part] + [n[:, :, None, :] for n in new_parts], axis=2)

    contexts = []
    final_cache = None
    for step_idx in range(steps):
        cache = cache_at(step_idx)
        if step_idx == steps - 1:
            final_cache = cache
        query = new_query[step_idx]
        scores = (
            jnp.einsum("rd,rpd->rp", query, cache[0], preferred_element_type=jnp.float32) * scaling
        )
        highest = jnp.max(scores, axis=1, keepdims=True)
        raw_weights = jnp.exp(scores - highest)
        totals = jnp.sum(raw_weights, axis=1, keepdims=True)
        summed = jnp.einsum(
            "rp,rpd->rd", raw_weights, cache[1].astype(jnp.float32), preferred_element_type=jnp.float32
        )
        contexts.append((summed / totals).astype(jnp.bfloat16))
    self_context = jnp.stack(contexts).reshape(steps * row_count, head_width)
    partial_out = jnp.dot(self_context, self_wo, preferred_element_type=jnp.float32)
    summed_out = lax.psum(partial_out.astype(jnp.bfloat16), "head").astype(jnp.float32)
    residual = hidden_in + summed_out.reshape(hidden_in.shape)
    normed_cross = rms_scaled(residual, cross_gain).astype(jnp.bfloat16)
    cross_query = jnp.dot(
        normed_cross.reshape(steps * row_count, -1), cross_wq, preferred_element_type=jnp.float32
    ).astype(jnp.bfloat16)
    by_doc = cross_query.reshape(steps, docs_here, TARGETS, head_width)

    sent = []
    for shift in range(BEAMS):
        route = [
            (beam * group_size + slot, slot * docs_here + (beam + shift) % BEAMS)
            for beam in range(BEAMS)
            for slot in range(group_size)
        ]
        piece = lax.dynamic_index_in_dim(by_doc, (my_beam + shift) % BEAMS, 1, keepdims=False)
        sent.append(lax.ppermute(piece, "hyp", route))
    doc_queries = jnp.stack(sent).reshape(BEAMS * steps * TARGETS, head_width)
    answer = cross_attend(doc_queries, cross_keys, cross_values, doc_length, scaling)
    answer = answer.reshape(BEAMS, steps, TARGETS, head_width)

    back = []
    for shift in range(BEAMS):
        route = [
            (slot * docs_here + (beam + shift) % BEAMS, beam * group_size + slot)
            for beam in range(BEAMS)
            for slot in range(group_size)
        ]
        back.append(lax.ppermute(answer[shift], "hyp", route))
    back = jnp.stack(back)
    order = (jnp.arange(docs_here, dtype=jnp.int32) - my_beam) % BEAMS
    by_k = jnp.take(back, order, axis=0)
    contexts_out = by_k.transpose(1, 0, 2, 3).reshape(steps, row_count, head_width)
    return (contexts_out, final_cache[0], final_cache[1])


def solution(mesh):
    return jax.shard_map(
        shards,
        mesh=mesh,
        in_specs=(
            P(None, "hyp", None),
            P(),
            P(),
            P(),
            P(None, "head"),
            P(None, "head"),
            P(None, "head"),
            P("head", None),
            P(),
            P(None, "head"),
            P("hyp", "head"),
            P("hyp", "head"),
            P("hyp"),
            P("hyp", None, "head"),
            P("hyp", None, "head"),
            P(),
        ),
        out_specs=(P(None, "hyp", "head"), P("hyp", None, "head"), P("hyp", None, "head")),
        check_vma=False,
    )
```

```python
import jax
import jax.numpy as jnp
from jax import lax
from jax.sharding import PartitionSpec as P


HEAD = 256
BEAMS = 4
TARGETS = 4


EPSILON = 1e-06


def rms_scaled(values_in, gain):
    mean_square = jnp.mean(values_in * values_in, axis=-1, keepdims=True)
    return values_in * lax.rsqrt(mean_square + EPSILON) * gain


def pick_rows(candidates, selector, row_axis):
    shape_list = [1] * candidates[0].ndim
    shape_list[row_axis] = selector.shape[0]
    chosen = candidates[0]
    for position in range(1, len(candidates)):
        chosen = jnp.where((selector == position).reshape(shape_list), candidates[position], chosen)
    return chosen


def beam_copies(block, hyp_count, group_size):
    copies = [block]
    for hop in range(1, BEAMS):
        distance = hop * group_size
        route = [((i - distance) % hyp_count, i) for i in range(hyp_count)]
        copies.append(lax.ppermute(block, "hyp", route))
    return copies


def ring_gather(block, axis):
    count = lax.axis_size(axis)
    me = lax.axis_index(axis)
    right = [(i, (i + 1) % count) for i in range(count)]
    left = [(i, (i - 1) % count) for i in range(count)]
    pieces = {0: block}
    from_left = block
    from_right = block
    for hop in range(1, count // 2):
        from_left = lax.ppermute(from_left, axis, right)
        from_right = lax.ppermute(from_right, axis, left)
        pieces[-hop] = from_left
        pieces[hop] = from_right
    if count % 2 == 0 and count > 1:
        half = block.shape[0] // 2
        top = lax.ppermute(from_left[:half], axis, right)
        bottom = lax.ppermute(from_right[half:], axis, left)
        pieces[count // 2] = jnp.concatenate([top, bottom], axis=0)
    ordered = jnp.stack([pieces[d] if d in pieces else pieces[d - count] for d in range(count // 2 - count + 1, count // 2 + 1)])
    first = (me + count // 2 - count + 1) % count
    order = (jnp.arange(count, dtype=jnp.int32) - first) % count
    by_device = jnp.take(ordered, order, axis=0)
    return by_device.transpose(1, 0, 2).reshape(block.shape[0], count * block.shape[1])


def cross_attend(queries, cross_keys, cross_values, doc_length, scaling):
    scores = (
        jnp.einsum("qd,jd->qj", queries, cross_keys, preferred_element_type=jnp.float32) * scaling
    )
    live_mask = lax.broadcasted_iota(jnp.int32, (1, cross_keys.shape[0]), 1) < doc_length
    scores = jnp.where(live_mask, scores, -jnp.inf)
    highest = jnp.max(scores, axis=1, keepdims=True)
    raw_weights = jnp.exp(scores - highest)
    totals = jnp.sum(raw_weights, axis=1, keepdims=True)
    weights = (raw_weights / totals).astype(jnp.bfloat16)
    output = jnp.einsum("qj,jd->qd", weights, cross_values, preferred_element_type=jnp.float32)
    return output.astype(jnp.bfloat16)


def shards(
    step_embeds,
    lang_table,
    lang_ids,
    self_gain,
    self_wq,
    self_wk,
    self_wv,
    self_wo,
    cross_gain,
    cross_wq,
    cross_wkv,
    encoder_rows,
    doc_lengths,
    past_keys,
    past_values,
    parents,
):
    hyp_count = lax.axis_size("hyp")
    group_size = hyp_count // BEAMS
    my_index = lax.axis_index("hyp")
    my_beam = my_index // group_size
    my_slot = my_index % group_size
    steps = step_embeds.shape[0]
    row_count = step_embeds.shape[1]
    docs_here = row_count // TARGETS
    head_width = self_wq.shape[1]
    doc_count = lang_ids.shape[0]
    scaling = HEAD ** (-0.5)

    full_weights = lax.all_gather(cross_wkv, "hyp", axis=0, tiled=True)
    full_rows = ring_gather(encoder_rows, "head")
    cross_kv = jnp.dot(full_rows, full_weights, preferred_element_type=jnp.float32).astype(
        jnp.bfloat16
    )
    cross_kv = cross_kv.reshape(encoder_rows.shape[0], 2, HEAD)
    cross_keys = cross_kv[:, 0, :]
    cross_values = cross_kv[:, 1, :]
    doc_length = doc_lengths[0]

    past_stack = jnp.stack([past_keys, past_values])
    past_all = beam_copies(past_stack, hyp_count, group_size)

    my_langs = lax.dynamic_slice_in_dim(lang_ids, my_slot * docs_here, docs_here, 0).reshape(row_count)
    one_hot = (
        my_langs[:, None] == lax.broadcasted_iota(jnp.int32, (1, lang_table.shape[0]), 1)
    ).astype(jnp.bfloat16)
    lang_rows = jnp.dot(one_hot, lang_table, preferred_element_type=jnp.float32)

    hidden_in = step_embeds.astype(jnp.float32) + lang_rows[None]
    normed = rms_scaled(hidden_in, self_gain).astype(jnp.bfloat16).reshape(steps * row_count, -1)
    new_query = jnp.dot(normed, self_wq, preferred_element_type=jnp.float32).astype(jnp.bfloat16)
    new_key = jnp.dot(normed, self_wk, preferred_element_type=jnp.float32).astype(jnp.bfloat16)
    new_value = jnp.dot(normed, self_wv, preferred_element_type=jnp.float32).astype(jnp.bfloat16)
    new_query = new_query.reshape(steps, row_count, head_width)
    fresh = jnp.stack([new_key, new_value]).reshape(2, steps, row_count, head_width)
    fresh_all = beam_copies(fresh, hyp_count, group_size)

    parent_view = parents.reshape(steps, BEAMS, doc_count * TARGETS)
    parent_of = lax.dynamic_slice_in_dim(parent_view, my_slot * row_count, row_count, 2)
    own_beam = jnp.full((row_count,), my_beam, jnp.int32)

    def hop_of(beam):
        return (my_beam - beam) % BEAMS

    def climb(step_idx, beam):
        return jnp.take_along_axis(parent_of[step_idx], beam[None, :], axis=0)[0]

    def cache_at(step_idx):
        ancestor = own_beam
        new_parts = [None] * (step_idx + 1)
        new_parts[step_idx] = fresh[:, step_idx]
        for back in range(step_idx, 0, -1):
            ancestor = climb(back, ancestor)
            new_parts[back - 1] = pick_rows(
                [f[:, back - 1] for f in fresh_all], hop_of(ancestor), 1
            )
        ancestor = climb(0, ancestor)
        past_part = pick_rows(past_all, hop_of(ancestor), 1)
        return jnp.concatenate([past_part] + [n[:, :, None, :] for n in new_parts], axis=2)

    contexts = []
    final_cache = None
    for step_idx in range(steps):
        cache = cache_at(step_idx)
        if step_idx == steps - 1:
            final_cache = cache
        query = new_query[step_idx]
        scores = (
            jnp.einsum("rd,rpd->rp", query, cache[0], preferred_element_type=jnp.float32) * scaling
        )
        highest = jnp.max(scores, axis=1, keepdims=True)
        raw_weights = jnp.exp(scores - highest)
        totals = jnp.sum(raw_weights, axis=1, keepdims=True)
        summed = jnp.einsum(
            "rp,rpd->rd", raw_weights, cache[1].astype(jnp.float32), preferred_element_type=jnp.float32
        )
        contexts.append((summed / totals).astype(jnp.bfloat16))
    self_context = jnp.stack(contexts).reshape(steps * row_count, head_width)
    partial_out = jnp.dot(self_context, self_wo, preferred_element_type=jnp.float32)
    summed_out = lax.psum(partial_out.astype(jnp.bfloat16), "head").astype(jnp.float32)
    residual = hidden_in + summed_out.reshape(hidden_in.shape)
    normed_cross = rms_scaled(residual, cross_gain).astype(jnp.bfloat16)
    cross_query = jnp.dot(
        normed_cross.reshape(steps * row_count, -1), cross_wq, preferred_element_type=jnp.float32
    ).astype(jnp.bfloat16)
    by_doc = cross_query.reshape(steps, docs_here, TARGETS, head_width)

    sent = []
    for shift in range(BEAMS):
        route = [
            (beam * group_size + slot, slot * docs_here + (beam + shift) % BEAMS)
            for beam in range(BEAMS)
            for slot in range(group_size)
        ]
        piece = lax.dynamic_index_in_dim(by_doc, (my_beam + shift) % BEAMS, 1, keepdims=False)
        sent.append(lax.ppermute(piece, "hyp", route))
    doc_queries = jnp.stack(sent).reshape(BEAMS * steps * TARGETS, head_width)
    answer = cross_attend(doc_queries, cross_keys, cross_values, doc_length, scaling)
    answer = answer.reshape(BEAMS, steps, TARGETS, head_width)

    back = []
    for shift in range(BEAMS):
        route = [
            (slot * docs_here + (beam + shift) % BEAMS, beam * group_size + slot)
            for beam in range(BEAMS)
            for slot in range(group_size)
        ]
        back.append(lax.ppermute(answer[shift], "hyp", route))
    back = jnp.stack(back)
    order = (jnp.arange(docs_here, dtype=jnp.int32) - my_beam) % BEAMS
    by_k = jnp.take(back, order, axis=0)
    contexts_out = by_k.transpose(1, 0, 2, 3).reshape(steps, row_count, head_width)
    return (contexts_out, final_cache[0], final_cache[1])


def solution(mesh):
    return jax.shard_map(
        shards,
        mesh=mesh,
        in_specs=(
            P(None, "hyp", None),
            P(),
            P(),
            P(),
            P(None, "head"),
            P(None, "head"),
            P(None, "head"),
            P("head", None),
            P(),
            P(None, "head"),
            P("hyp", "head"),
            P("hyp", "head"),
            P("hyp"),
            P("hyp", None, "head"),
            P("hyp", None, "head"),
            P(),
        ),
        out_specs=(P(None, "hyp", "head"), P("hyp", None, "head"), P("hyp", None, "head")),
        check_vma=False,
    )
```

```python
import jax
import jax.numpy as jnp
from jax import lax
from jax.sharding import PartitionSpec as P


HEAD = 256
BEAMS = 4
TARGETS = 4


EPSILON = 1e-06


def rms_scaled(values_in, gain):
    mean_square = jnp.mean(values_in * values_in, axis=-1, keepdims=True)
    return values_in * lax.rsqrt(mean_square + EPSILON) * gain


def pick_rows(candidates, selector, row_axis):
    shape_list = [1] * candidates[0].ndim
    shape_list[row_axis] = selector.shape[0]
    chosen = candidates[0]
    for position in range(1, len(candidates)):
        chosen = jnp.where((selector == position).reshape(shape_list), candidates[position], chosen)
    return chosen


def beam_copies(block, hyp_count, group_size):
    copies = [block]
    for hop in range(1, BEAMS):
        distance = hop * group_size
        route = [((i - distance) % hyp_count, i) for i in range(hyp_count)]
        copies.append(lax.ppermute(block, "hyp", route))
    return copies


def ring_project(block, weights, axis):
    count = lax.axis_size(axis)
    me = lax.axis_index(axis)
    width = block.shape[1]
    right = [(i, (i + 1) % count) for i in range(count)]
    left = [(i, (i - 1) % count) for i in range(count)]

    def partial(piece, offset):
        source = (me + offset) % count
        w = lax.dynamic_slice_in_dim(weights, source * width, width, 0)
        return jnp.dot(piece, w, preferred_element_type=jnp.float32)

    total = partial(block, 0)
    from_left = block
    from_right = block
    for hop in range(1, count // 2):
        from_left = lax.ppermute(from_left, axis, right)
        from_right = lax.ppermute(from_right, axis, left)
        total = total + partial(from_left, -hop) + partial(from_right, hop)
    if count % 2 == 0 and count > 1:
        half = block.shape[0] // 2
        top = lax.ppermute(from_left[:half], axis, right)
        bottom = lax.ppermute(from_right[half:], axis, left)
        last = jnp.concatenate([top, bottom], axis=0)
        total = total + partial(last, count // 2)
    return total


def cross_attend(queries, cross_keys, cross_values, doc_length, scaling):
    scores = (
        jnp.einsum("qd,jd->qj", queries, cross_keys, preferred_element_type=jnp.float32) * scaling
    )
    live_mask = lax.broadcasted_iota(jnp.int32, (1, cross_keys.shape[0]), 1) < doc_length
    scores = jnp.where(live_mask, scores, -jnp.inf)
    highest = jnp.max(scores, axis=1, keepdims=True)
    raw_weights = jnp.exp(scores - highest)
    totals = jnp.sum(raw_weights, axis=1, keepdims=True)
    weights = (raw_weights / totals).astype(jnp.bfloat16)
    output = jnp.einsum("qj,jd->qd", weights, cross_values, preferred_element_type=jnp.float32)
    return output.astype(jnp.bfloat16)


def shards(
    step_embeds,
    lang_table,
    lang_ids,
    self_gain,
    self_wq,
    self_wk,
    self_wv,
    self_wo,
    cross_gain,
    cross_wq,
    cross_wkv,
    encoder_rows,
    doc_lengths,
    past_keys,
    past_values,
    parents,
):
    hyp_count = lax.axis_size("hyp")
    group_size = hyp_count // BEAMS
    my_index = lax.axis_index("hyp")
    my_beam = my_index // group_size
    my_slot = my_index % group_size
    steps = step_embeds.shape[0]
    row_count = step_embeds.shape[1]
    docs_here = row_count // TARGETS
    head_width = self_wq.shape[1]
    doc_count = lang_ids.shape[0]
    scaling = HEAD ** (-0.5)

    full_weights = lax.all_gather(cross_wkv, "hyp", axis=0, tiled=True)
    cross_kv = ring_project(encoder_rows, full_weights, "head").astype(jnp.bfloat16)
    cross_kv = cross_kv.reshape(encoder_rows.shape[0], 2, HEAD)
    cross_keys = cross_kv[:, 0, :]
    cross_values = cross_kv[:, 1, :]
    doc_length = doc_lengths[0]

    past_stack = jnp.stack([past_keys, past_values])
    past_all = beam_copies(past_stack, hyp_count, group_size)

    my_langs = lax.dynamic_slice_in_dim(lang_ids, my_slot * docs_here, docs_here, 0).reshape(row_count)
    one_hot = (
        my_langs[:, None] == lax.broadcasted_iota(jnp.int32, (1, lang_table.shape[0]), 1)
    ).astype(jnp.bfloat16)
    lang_rows = jnp.dot(one_hot, lang_table, preferred_element_type=jnp.float32)

    hidden_in = step_embeds.astype(jnp.float32) + lang_rows[None]
    normed = rms_scaled(hidden_in, self_gain).astype(jnp.bfloat16).reshape(steps * row_count, -1)
    new_query = jnp.dot(normed, self_wq, preferred_element_type=jnp.float32).astype(jnp.bfloat16)
    new_key = jnp.dot(normed, self_wk, preferred_element_type=jnp.float32).astype(jnp.bfloat16)
    new_value = jnp.dot(normed, self_wv, preferred_element_type=jnp.float32).astype(jnp.bfloat16)
    new_query = new_query.reshape(steps, row_count, head_width)
    fresh = jnp.stack([new_key, new_value]).reshape(2, steps, row_count, head_width)
    fresh_all = beam_copies(fresh, hyp_count, group_size)

    parent_view = parents.reshape(steps, BEAMS, doc_count * TARGETS)
    parent_of = lax.dynamic_slice_in_dim(parent_view, my_slot * row_count, row_count, 2)
    own_beam = jnp.full((row_count,), my_beam, jnp.int32)

    def hop_of(beam):
        return (my_beam - beam) % BEAMS

    def climb(step_idx, beam):
        return jnp.take_along_axis(parent_of[step_idx], beam[None, :], axis=0)[0]

    def cache_at(step_idx):
        ancestor = own_beam
        new_parts = [None] * (step_idx + 1)
        new_parts[step_idx] = fresh[:, step_idx]
        for back in range(step_idx, 0, -1):
            ancestor = climb(back, ancestor)
            new_parts[back - 1] = pick_rows(
                [f[:, back - 1] for f in fresh_all], hop_of(ancestor), 1
            )
        ancestor = climb(0, ancestor)
        past_part = pick_rows(past_all, hop_of(ancestor), 1)
        return jnp.concatenate([past_part] + [n[:, :, None, :] for n in new_parts], axis=2)

    contexts = []
    final_cache = None
    for step_idx in range(steps):
        cache = cache_at(step_idx)
        if step_idx == steps - 1:
            final_cache = cache
        query = new_query[step_idx]
        scores = (
            jnp.einsum("rd,rpd->rp", query, cache[0], preferred_element_type=jnp.float32)
            * scaling
        )
        highest = jnp.max(scores, axis=1, keepdims=True)
        raw_weights = jnp.exp(scores - highest)
        totals = jnp.sum(raw_weights, axis=1, keepdims=True)
        summed = jnp.einsum(
            "rp,rpd->rd",
            raw_weights,
            cache[1].astype(jnp.float32),
            preferred_element_type=jnp.float32,
        )
        contexts.append((summed / totals).astype(jnp.bfloat16))
    self_context = jnp.stack(contexts).reshape(steps * row_count, head_width)
    partial_out = jnp.dot(self_context, self_wo, preferred_element_type=jnp.float32)
    every_part = lax.all_gather(partial_out.astype(jnp.bfloat16), "head", axis=0, tiled=False)
    summed_out = jnp.sum(every_part.astype(jnp.float32), axis=0)
    residual = hidden_in + summed_out.reshape(hidden_in.shape)
    normed_cross = rms_scaled(residual, cross_gain).astype(jnp.bfloat16)
    cross_query = jnp.dot(
        normed_cross.reshape(steps * row_count, -1), cross_wq, preferred_element_type=jnp.float32
    ).astype(jnp.bfloat16)
    by_doc = cross_query.reshape(steps, docs_here, TARGETS, head_width)

    sent = []
    for shift in range(BEAMS):
        route = [
            (beam * group_size + slot, slot * docs_here + (beam + shift) % BEAMS)
            for beam in range(BEAMS)
            for slot in range(group_size)
        ]
        piece = lax.dynamic_index_in_dim(by_doc, (my_beam + shift) % BEAMS, 1, keepdims=False)
        sent.append(lax.ppermute(piece, "hyp", route))
    doc_queries = jnp.stack(sent).reshape(BEAMS * steps * TARGETS, head_width)
    answer = cross_attend(doc_queries, cross_keys, cross_values, doc_length, scaling)
    answer = answer.reshape(BEAMS, steps, TARGETS, head_width)

    back = []
    for shift in range(BEAMS):
        route = [
            (slot * docs_here + (beam + shift) % BEAMS, beam * group_size + slot)
            for beam in range(BEAMS)
            for slot in range(group_size)
        ]
        back.append(lax.ppermute(answer[shift], "hyp", route))
    back = jnp.stack(back)
    order = (jnp.arange(docs_here, dtype=jnp.int32) - my_beam) % BEAMS
    by_k = jnp.take(back, order, axis=0)
    contexts_out = by_k.transpose(1, 0, 2, 3).reshape(steps, row_count, head_width)
    return (contexts_out, final_cache[0], final_cache[1])


def solution(mesh):
    return jax.shard_map(
        shards,
        mesh=mesh,
        in_specs=(
            P(None, "hyp", None),
            P(),
            P(),
            P(),
            P(None, "head"),
            P(None, "head"),
            P(None, "head"),
            P("head", None),
            P(),
            P(None, "head"),
            P("hyp", "head"),
            P("hyp", "head"),
            P("hyp"),
            P("hyp", None, "head"),
            P("hyp", None, "head"),
            P(),
        ),
        out_specs=(P(None, "hyp", "head"), P("hyp", None, "head"), P("hyp", None, "head")),
        check_vma=False,
    )
```

```python
import jax
import jax.numpy as jnp
from jax import lax
from jax.sharding import PartitionSpec as P


HEAD = 256
BEAMS = 4
TARGETS = 4


EPSILON = 1e-06


def rms_scaled(values_in, gain):
    mean_square = jnp.mean(values_in * values_in, axis=-1, keepdims=True)
    return values_in * lax.rsqrt(mean_square + EPSILON) * gain


def pick_rows(candidates, selector, row_axis):
    shape_list = [1] * candidates[0].ndim
    shape_list[row_axis] = selector.shape[0]
    chosen = candidates[0]
    for position in range(1, len(candidates)):
        chosen = jnp.where((selector == position).reshape(shape_list), candidates[position], chosen)
    return chosen


def beam_copies(block, hyp_count, group_size):
    copies = [block]
    for hop in range(1, BEAMS):
        distance = hop * group_size
        route = [((i - distance) % hyp_count, i) for i in range(hyp_count)]
        copies.append(lax.ppermute(block, "hyp", route))
    return copies


def ring_project(block, weights, axis):
    count = lax.axis_size(axis)
    me = lax.axis_index(axis)
    width = block.shape[1]
    right = [(i, (i + 1) % count) for i in range(count)]
    left = [(i, (i - 1) % count) for i in range(count)]

    def partial(piece, offset):
        source = (me + offset) % count
        w = lax.dynamic_slice_in_dim(weights, source * width, width, 0)
        return jnp.dot(piece, w, preferred_element_type=jnp.float32)

    total = partial(block, 0)
    from_left = block
    from_right = block
    for hop in range(1, count // 2):
        from_left = lax.ppermute(from_left, axis, right)
        from_right = lax.ppermute(from_right, axis, left)
        total = total + partial(from_left, -hop) + partial(from_right, hop)
    if count % 2 == 0 and count > 1:
        half = block.shape[0] // 2
        top = lax.ppermute(from_left[:half], axis, right)
        bottom = lax.ppermute(from_right[half:], axis, left)
        last = jnp.concatenate([top, bottom], axis=0)
        total = total + partial(last, count // 2)
    return total


def cross_attend(queries, cross_keys, cross_values, doc_length, scaling):
    scores = (
        jnp.einsum("qd,jd->qj", queries, cross_keys, preferred_element_type=jnp.float32) * scaling
    )
    live_mask = lax.broadcasted_iota(jnp.int32, (1, cross_keys.shape[0]), 1) < doc_length
    scores = jnp.where(live_mask, scores, -jnp.inf)
    highest = jnp.max(scores, axis=1, keepdims=True)
    raw_weights = jnp.exp(scores - highest)
    totals = jnp.sum(raw_weights, axis=1, keepdims=True)
    weights = (raw_weights / totals).astype(jnp.bfloat16)
    output = jnp.einsum("qj,jd->qd", weights, cross_values, preferred_element_type=jnp.float32)
    return output.astype(jnp.bfloat16)


def shards(
    step_embeds,
    lang_table,
    lang_ids,
    self_gain,
    self_wq,
    self_wk,
    self_wv,
    self_wo,
    cross_gain,
    cross_wq,
    cross_wkv,
    encoder_rows,
    doc_lengths,
    past_keys,
    past_values,
    parents,
):
    hyp_count = lax.axis_size("hyp")
    group_size = hyp_count // BEAMS
    my_index = lax.axis_index("hyp")
    my_beam = my_index // group_size
    my_slot = my_index % group_size
    steps = step_embeds.shape[0]
    row_count = step_embeds.shape[1]
    docs_here = row_count // TARGETS
    head_width = self_wq.shape[1]
    doc_count = lang_ids.shape[0]
    scaling = HEAD ** (-0.5)

    full_weights = lax.all_gather(cross_wkv, "hyp", axis=0, tiled=True)
    cross_kv = ring_project(encoder_rows, full_weights, "head").astype(jnp.bfloat16)
    cross_kv = cross_kv.reshape(encoder_rows.shape[0], 2, HEAD)
    cross_keys = cross_kv[:, 0, :]
    cross_values = cross_kv[:, 1, :]
    doc_length = doc_lengths[0]

    past_stack = jnp.stack([past_keys, past_values])
    past_all = beam_copies(past_stack, hyp_count, group_size)

    my_langs = lax.dynamic_slice_in_dim(lang_ids, my_slot * docs_here, docs_here, 0).reshape(row_count)
    one_hot = (
        my_langs[:, None] == lax.broadcasted_iota(jnp.int32, (1, lang_table.shape[0]), 1)
    ).astype(jnp.bfloat16)
    lang_rows = jnp.dot(one_hot, lang_table, preferred_element_type=jnp.float32)

    hidden_in = step_embeds.astype(jnp.float32) + lang_rows[None]
    normed = rms_scaled(hidden_in, self_gain).astype(jnp.bfloat16).reshape(steps * row_count, -1)
    new_query = jnp.dot(normed, self_wq, preferred_element_type=jnp.float32).astype(jnp.bfloat16)
    new_key = jnp.dot(normed, self_wk, preferred_element_type=jnp.float32).astype(jnp.bfloat16)
    new_value = jnp.dot(normed, self_wv, preferred_element_type=jnp.float32).astype(jnp.bfloat16)
    new_query = new_query.reshape(steps, row_count, head_width)
    fresh = jnp.stack([new_key, new_value]).reshape(2, steps, row_count, head_width)
    fresh_all = beam_copies(fresh, hyp_count, group_size)

    parent_view = parents.reshape(steps, BEAMS, doc_count * TARGETS)
    parent_of = lax.dynamic_slice_in_dim(parent_view, my_slot * row_count, row_count, 2)
    own_beam = jnp.full((row_count,), my_beam, jnp.int32)

    def hop_of(beam):
        return (my_beam - beam) % BEAMS

    def climb(step_idx, beam):
        return jnp.take_along_axis(parent_of[step_idx], beam[None, :], axis=0)[0]

    def cache_at(step_idx):
        ancestor = own_beam
        new_parts = [None] * (step_idx + 1)
        new_parts[step_idx] = fresh[:, step_idx]
        for back in range(step_idx, 0, -1):
            ancestor = climb(back, ancestor)
            new_parts[back - 1] = pick_rows(
                [f[:, back - 1] for f in fresh_all], hop_of(ancestor), 1
            )
        ancestor = climb(0, ancestor)
        past_part = pick_rows(past_all, hop_of(ancestor), 1)
        return jnp.concatenate([past_part] + [n[:, :, None, :] for n in new_parts], axis=2)

    contexts = []
    final_cache = None
    for step_idx in range(steps):
        cache = cache_at(step_idx)
        if step_idx == steps - 1:
            final_cache = cache
        query = new_query[step_idx]
        scores = (
            jnp.einsum("rd,rpd->rp", query, cache[0], preferred_element_type=jnp.float32)
            * scaling
        )
        highest = jnp.max(scores, axis=1, keepdims=True)
        raw_weights = jnp.exp(scores - highest)
        totals = jnp.sum(raw_weights, axis=1, keepdims=True)
        summed = jnp.einsum(
            "rp,rpd->rd",
            raw_weights,
            cache[1].astype(jnp.float32),
            preferred_element_type=jnp.float32,
        )
        contexts.append((summed / totals).astype(jnp.bfloat16))
    self_context = jnp.stack(contexts).reshape(steps * row_count, head_width)
    partial_out = jnp.dot(self_context, self_wo, preferred_element_type=jnp.float32)
    block_sum = lax.psum_scatter(
        partial_out.astype(jnp.bfloat16), "head", scatter_dimension=1, tiled=True
    )
    summed_out = lax.all_gather(block_sum, "head", axis=1, tiled=True).astype(jnp.float32)
    residual = hidden_in + summed_out.reshape(hidden_in.shape)
    normed_cross = rms_scaled(residual, cross_gain).astype(jnp.bfloat16)
    cross_query = jnp.dot(
        normed_cross.reshape(steps * row_count, -1), cross_wq, preferred_element_type=jnp.float32
    ).astype(jnp.bfloat16)
    by_doc = cross_query.reshape(steps, docs_here, TARGETS, head_width)

    sent = []
    for shift in range(BEAMS):
        route = [
            (beam * group_size + slot, slot * docs_here + (beam + shift) % BEAMS)
            for beam in range(BEAMS)
            for slot in range(group_size)
        ]
        piece = lax.dynamic_index_in_dim(by_doc, (my_beam + shift) % BEAMS, 1, keepdims=False)
        sent.append(lax.ppermute(piece, "hyp", route))
    doc_queries = jnp.stack(sent).reshape(BEAMS * steps * TARGETS, head_width)
    answer = cross_attend(doc_queries, cross_keys, cross_values, doc_length, scaling)
    answer = answer.reshape(BEAMS, steps, TARGETS, head_width)

    back = []
    for shift in range(BEAMS):
        route = [
            (slot * docs_here + (beam + shift) % BEAMS, beam * group_size + slot)
            for beam in range(BEAMS)
            for slot in range(group_size)
        ]
        back.append(lax.ppermute(answer[shift], "hyp", route))
    back = jnp.stack(back)
    order = (jnp.arange(docs_here, dtype=jnp.int32) - my_beam) % BEAMS
    by_k = jnp.take(back, order, axis=0)
    contexts_out = by_k.transpose(1, 0, 2, 3).reshape(steps, row_count, head_width)
    return (contexts_out, final_cache[0], final_cache[1])


def solution(mesh):
    return jax.shard_map(
        shards,
        mesh=mesh,
        in_specs=(
            P(None, "hyp", None),
            P(),
            P(),
            P(),
            P(None, "head"),
            P(None, "head"),
            P(None, "head"),
            P("head", None),
            P(),
            P(None, "head"),
            P("hyp", "head"),
            P("hyp", "head"),
            P("hyp"),
            P("hyp", None, "head"),
            P("hyp", None, "head"),
            P(),
        ),
        out_specs=(P(None, "hyp", "head"), P("hyp", None, "head"), P("hyp", None, "head")),
        check_vma=False,
    )
```

```python
import jax
import jax.numpy as jnp
from jax import lax
from jax.sharding import PartitionSpec as P


HEAD = 256
BEAMS = 4
TARGETS = 4


EPSILON = 1e-06


def rms_scaled(values_in, gain):
    mean_square = jnp.mean(values_in * values_in, axis=-1, keepdims=True)
    return values_in * lax.rsqrt(mean_square + EPSILON) * gain


def pick_rows(candidates, selector, row_axis):
    shape_list = [1] * candidates[0].ndim
    shape_list[row_axis] = selector.shape[0]
    chosen = candidates[0]
    for position in range(1, len(candidates)):
        chosen = jnp.where((selector == position).reshape(shape_list), candidates[position], chosen)
    return chosen


def beam_copies(block, hyp_count, group_size):
    copies = [block]
    for hop in range(1, BEAMS):
        distance = hop * group_size
        route = [((i - distance) % hyp_count, i) for i in range(hyp_count)]
        copies.append(lax.ppermute(block, "hyp", route))
    return copies


def ring_project(block, weights, axis):
    count = lax.axis_size(axis)
    me = lax.axis_index(axis)
    width = block.shape[1]
    right = [(i, (i + 1) % count) for i in range(count)]
    left = [(i, (i - 1) % count) for i in range(count)]

    def partial(piece, offset):
        source = (me + offset) % count
        w = lax.dynamic_slice_in_dim(weights, source * width, width, 0)
        return jnp.dot(piece, w, preferred_element_type=jnp.float32)

    total = partial(block, 0)
    from_left = block
    from_right = block
    for hop in range(1, count // 2):
        from_left = lax.ppermute(from_left, axis, right)
        from_right = lax.ppermute(from_right, axis, left)
        total = total + partial(from_left, -hop) + partial(from_right, hop)
    if count % 2 == 0 and count > 1:
        half = block.shape[0] // 2
        top = lax.ppermute(from_left[:half], axis, right)
        bottom = lax.ppermute(from_right[half:], axis, left)
        last = jnp.concatenate([top, bottom], axis=0)
        total = total + partial(last, count // 2)
    return total


def cross_attend(queries, cross_keys, cross_values, doc_length, scaling):
    scores = (
        jnp.einsum("qd,jd->qj", queries, cross_keys, preferred_element_type=jnp.float32) * scaling
    )
    live_mask = lax.broadcasted_iota(jnp.int32, (1, cross_keys.shape[0]), 1) < doc_length
    scores = jnp.where(live_mask, scores, -jnp.inf)
    highest = jnp.max(scores, axis=1, keepdims=True)
    raw_weights = jnp.exp(scores - highest)
    totals = jnp.sum(raw_weights, axis=1, keepdims=True)
    weights = (raw_weights / totals).astype(jnp.bfloat16)
    output = jnp.einsum("qj,jd->qd", weights, cross_values, preferred_element_type=jnp.float32)
    return output.astype(jnp.bfloat16)


def shards(
    step_embeds,
    lang_table,
    lang_ids,
    self_gain,
    self_wq,
    self_wk,
    self_wv,
    self_wo,
    cross_gain,
    cross_wq,
    cross_wkv,
    encoder_rows,
    doc_lengths,
    past_keys,
    past_values,
    parents,
):
    hyp_count = lax.axis_size("hyp")
    group_size = hyp_count // BEAMS
    my_index = lax.axis_index("hyp")
    my_beam = my_index // group_size
    my_slot = my_index % group_size
    steps = step_embeds.shape[0]
    row_count = step_embeds.shape[1]
    docs_here = row_count // TARGETS
    head_width = self_wq.shape[1]
    doc_count = lang_ids.shape[0]
    scaling = HEAD ** (-0.5)

    full_weights = lax.all_gather(cross_wkv, "hyp", axis=0, tiled=True)
    cross_kv = ring_project(encoder_rows, full_weights, "head").astype(jnp.bfloat16)
    cross_kv = cross_kv.reshape(encoder_rows.shape[0], 2, HEAD)
    cross_keys = cross_kv[:, 0, :]
    cross_values = cross_kv[:, 1, :]
    doc_length = doc_lengths[0]

    past_stack = jnp.stack([past_keys, past_values])
    past_all = beam_copies(past_stack, hyp_count, group_size)

    my_langs = lax.dynamic_slice_in_dim(lang_ids, my_slot * docs_here, docs_here, 0).reshape(row_count)
    one_hot = (
        my_langs[:, None] == lax.broadcasted_iota(jnp.int32, (1, lang_table.shape[0]), 1)
    ).astype(jnp.bfloat16)
    lang_rows = jnp.dot(one_hot, lang_table, preferred_element_type=jnp.float32)

    hidden_in = step_embeds.astype(jnp.float32) + lang_rows[None]
    normed = rms_scaled(hidden_in, self_gain).astype(jnp.bfloat16)
    normed = normed.reshape(steps * row_count, -1)
    new_query = jnp.dot(normed, self_wq, preferred_element_type=jnp.float32)
    new_key = jnp.dot(normed, self_wk, preferred_element_type=jnp.float32)
    new_value = jnp.dot(normed, self_wv, preferred_element_type=jnp.float32)
    new_query = new_query.astype(jnp.bfloat16)
    new_key = new_key.astype(jnp.bfloat16)
    new_value = new_value.astype(jnp.bfloat16)
    new_query = new_query.reshape(steps, row_count, head_width)
    fresh = jnp.stack([new_key, new_value]).reshape(2, steps, row_count, head_width)
    fresh_all = beam_copies(fresh, hyp_count, group_size)

    parent_view = parents.reshape(steps, BEAMS, doc_count * TARGETS)
    parent_of = lax.dynamic_slice_in_dim(parent_view, my_slot * row_count, row_count, 2)
    own_beam = jnp.full((row_count,), my_beam, jnp.int32)

    def hop_of(beam):
        return (my_beam - beam) % BEAMS

    def climb(step_idx, beam):
        return jnp.take_along_axis(parent_of[step_idx], beam[None, :], axis=0)[0]

    def cache_at(step_idx):
        ancestor = own_beam
        new_parts = [None] * (step_idx + 1)
        new_parts[step_idx] = fresh[:, step_idx]
        for back in range(step_idx, 0, -1):
            ancestor = climb(back, ancestor)
            new_parts[back - 1] = pick_rows(
                [f[:, back - 1] for f in fresh_all], hop_of(ancestor), 1
            )
        ancestor = climb(0, ancestor)
        past_part = pick_rows(past_all, hop_of(ancestor), 1)
        return jnp.concatenate([past_part] + [n[:, :, None, :] for n in new_parts], axis=2)

    contexts = []
    final_cache = None
    for step_idx in range(steps):
        cache = cache_at(step_idx)
        if step_idx == steps - 1:
            final_cache = cache
        query = new_query[step_idx]
        scores = (
            jnp.einsum("rd,rpd->rp", query, cache[0], preferred_element_type=jnp.float32)
            * scaling
        )
        highest = jnp.max(scores, axis=1, keepdims=True)
        raw_weights = jnp.exp(scores - highest)
        totals = jnp.sum(raw_weights, axis=1, keepdims=True)
        summed = jnp.einsum(
            "rp,rpd->rd",
            raw_weights,
            cache[1].astype(jnp.float32),
            preferred_element_type=jnp.float32,
        )
        contexts.append((summed / totals).astype(jnp.bfloat16))
    self_context = jnp.stack(contexts).reshape(steps * row_count, head_width)
    partial_out = jnp.dot(self_context, self_wo, preferred_element_type=jnp.float32)
    every_part = lax.all_gather(partial_out.astype(jnp.bfloat16), "head", axis=0, tiled=False)
    summed_out = jnp.sum(every_part.astype(jnp.float32), axis=0)
    residual = hidden_in + summed_out.reshape(hidden_in.shape)
    normed_cross = rms_scaled(residual, cross_gain).astype(jnp.bfloat16)
    cross_query = jnp.dot(
        normed_cross.reshape(steps * row_count, -1), cross_wq, preferred_element_type=jnp.float32
    ).astype(jnp.bfloat16)
    by_doc = cross_query.reshape(steps, docs_here, TARGETS, head_width)

    sent = []
    for shift in range(BEAMS):
        route = [
            (beam * group_size + slot, slot * docs_here + (beam + shift) % BEAMS)
            for beam in range(BEAMS)
            for slot in range(group_size)
        ]
        piece = lax.dynamic_index_in_dim(by_doc, (my_beam + shift) % BEAMS, 1, keepdims=False)
        sent.append(lax.ppermute(piece, "hyp", route))
    doc_queries = jnp.stack(sent).reshape(BEAMS * steps * TARGETS, head_width)
    answer = cross_attend(doc_queries, cross_keys, cross_values, doc_length, scaling)
    answer = answer.reshape(BEAMS, steps, TARGETS, head_width)

    back = []
    for shift in range(BEAMS):
        route = [
            (slot * docs_here + (beam + shift) % BEAMS, beam * group_size + slot)
            for beam in range(BEAMS)
            for slot in range(group_size)
        ]
        back.append(lax.ppermute(answer[shift], "hyp", route))
    back = jnp.stack(back)
    order = (jnp.arange(docs_here, dtype=jnp.int32) - my_beam) % BEAMS
    by_k = jnp.take(back, order, axis=0)
    contexts_out = by_k.transpose(1, 0, 2, 3).reshape(steps, row_count, head_width)
    return (contexts_out, final_cache[0], final_cache[1])


def solution(mesh):
    return jax.shard_map(
        shards,
        mesh=mesh,
        in_specs=(
            P(None, "hyp", None),
            P(),
            P(),
            P(),
            P(None, "head"),
            P(None, "head"),
            P(None, "head"),
            P("head", None),
            P(),
            P(None, "head"),
            P("hyp", "head"),
            P("hyp", "head"),
            P("hyp"),
            P("hyp", None, "head"),
            P("hyp", None, "head"),
            P(),
        ),
        out_specs=(P(None, "hyp", "head"), P("hyp", None, "head"), P("hyp", None, "head")),
        check_vma=False,
    )
```

```python
import jax
import jax.numpy as jnp
from jax import lax
from jax.sharding import PartitionSpec as P


HEAD = 256
BEAMS = 4
TARGETS = 4


EPSILON = 1e-06


def rms_scaled(values_in, gain):
    mean_square = jnp.mean(values_in * values_in, axis=-1, keepdims=True)
    return values_in * lax.rsqrt(mean_square + EPSILON) * gain


def pick_rows(candidates, selector, row_axis):
    shape_list = [1] * candidates[0].ndim
    shape_list[row_axis] = selector.shape[0]
    chosen = candidates[0]
    for position in range(1, len(candidates)):
        chosen = jnp.where((selector == position).reshape(shape_list), candidates[position], chosen)
    return chosen


def beam_copies(block, hyp_count, group_size):
    copies = [block]
    for hop in range(1, BEAMS):
        distance = hop * group_size
        route = [((i - distance) % hyp_count, i) for i in range(hyp_count)]
        copies.append(lax.ppermute(block, "hyp", route))
    return copies


def ring_project(block, weights, axis):
    count = lax.axis_size(axis)
    me = lax.axis_index(axis)
    width = block.shape[1]
    right = [(i, (i + 1) % count) for i in range(count)]
    left = [(i, (i - 1) % count) for i in range(count)]

    def partial(piece, offset):
        source = (me + offset) % count
        w = lax.dynamic_slice_in_dim(weights, source * width, width, 0)
        return jnp.dot(piece, w, preferred_element_type=jnp.float32)

    total = partial(block, 0)
    from_left = block
    from_right = block
    for hop in range(1, count // 2):
        from_left = lax.ppermute(from_left, axis, right)
        from_right = lax.ppermute(from_right, axis, left)
        total = total + partial(from_left, -hop) + partial(from_right, hop)
    if count % 2 == 0 and count > 1:
        half = block.shape[0] // 2
        top = lax.ppermute(from_left[:half], axis, right)
        bottom = lax.ppermute(from_right[half:], axis, left)
        last = jnp.concatenate([top, bottom], axis=0)
        total = total + partial(last, count // 2)
    return total


def ring_sum(block, axis):
    count = lax.axis_size(axis)
    right = [(i, (i + 1) % count) for i in range(count)]
    left = [(i, (i - 1) % count) for i in range(count)]
    total = block.astype(jnp.float32)
    from_left = block
    from_right = block
    for _ in range(1, count // 2):
        from_left = lax.ppermute(from_left, axis, right)
        from_right = lax.ppermute(from_right, axis, left)
        total = total + from_left.astype(jnp.float32) + from_right.astype(jnp.float32)
    if count % 2 == 0 and count > 1:
        half = block.shape[0] // 2
        top = lax.ppermute(from_left[:half], axis, right)
        bottom = lax.ppermute(from_right[half:], axis, left)
        total = total + jnp.concatenate([top, bottom], axis=0).astype(jnp.float32)
    return total


def cross_attend(queries, cross_keys, cross_values, doc_length, scaling):
    scores = (
        jnp.einsum("qd,jd->qj", queries, cross_keys, preferred_element_type=jnp.float32) * scaling
    )
    live_mask = lax.broadcasted_iota(jnp.int32, (1, cross_keys.shape[0]), 1) < doc_length
    scores = jnp.where(live_mask, scores, -jnp.inf)
    highest = jnp.max(scores, axis=1, keepdims=True)
    raw_weights = jnp.exp(scores - highest)
    totals = jnp.sum(raw_weights, axis=1, keepdims=True)
    weights = (raw_weights / totals).astype(jnp.bfloat16)
    output = jnp.einsum("qj,jd->qd", weights, cross_values, preferred_element_type=jnp.float32)
    return output.astype(jnp.bfloat16)


def shards(
    step_embeds,
    lang_table,
    lang_ids,
    self_gain,
    self_wq,
    self_wk,
    self_wv,
    self_wo,
    cross_gain,
    cross_wq,
    cross_wkv,
    encoder_rows,
    doc_lengths,
    past_keys,
    past_values,
    parents,
):
    hyp_count = lax.axis_size("hyp")
    group_size = hyp_count // BEAMS
    my_index = lax.axis_index("hyp")
    my_beam = my_index // group_size
    my_slot = my_index % group_size
    steps = step_embeds.shape[0]
    row_count = step_embeds.shape[1]
    docs_here = row_count // TARGETS
    head_width = self_wq.shape[1]
    doc_count = lang_ids.shape[0]
    scaling = HEAD ** (-0.5)

    full_weights = lax.all_gather(cross_wkv, "hyp", axis=0, tiled=True)
    cross_kv = ring_project(encoder_rows, full_weights, "head").astype(jnp.bfloat16)
    cross_kv = cross_kv.reshape(encoder_rows.shape[0], 2, HEAD)
    cross_keys = cross_kv[:, 0, :]
    cross_values = cross_kv[:, 1, :]
    doc_length = doc_lengths[0]

    past_stack = jnp.stack([past_keys, past_values])
    past_all = beam_copies(past_stack, hyp_count, group_size)

    my_langs = lax.dynamic_slice_in_dim(lang_ids, my_slot * docs_here, docs_here, 0).reshape(row_count)
    one_hot = (
        my_langs[:, None] == lax.broadcasted_iota(jnp.int32, (1, lang_table.shape[0]), 1)
    ).astype(jnp.bfloat16)
    lang_rows = jnp.dot(one_hot, lang_table, preferred_element_type=jnp.float32)

    hidden_in = step_embeds.astype(jnp.float32) + lang_rows[None]
    normed = rms_scaled(hidden_in, self_gain).astype(jnp.bfloat16)
    normed = normed.reshape(steps * row_count, -1)
    new_query = jnp.dot(normed, self_wq, preferred_element_type=jnp.float32)
    new_key = jnp.dot(normed, self_wk, preferred_element_type=jnp.float32)
    new_value = jnp.dot(normed, self_wv, preferred_element_type=jnp.float32)
    new_query = new_query.astype(jnp.bfloat16)
    new_key = new_key.astype(jnp.bfloat16)
    new_value = new_value.astype(jnp.bfloat16)
    new_query = new_query.reshape(steps, row_count, head_width)
    fresh = jnp.stack([new_key, new_value]).reshape(2, steps, row_count, head_width)
    fresh_all = beam_copies(fresh, hyp_count, group_size)

    parent_view = parents.reshape(steps, BEAMS, doc_count * TARGETS)
    parent_of = lax.dynamic_slice_in_dim(parent_view, my_slot * row_count, row_count, 2)
    own_beam = jnp.full((row_count,), my_beam, jnp.int32)

    def hop_of(beam):
        return (my_beam - beam) % BEAMS

    def climb(step_idx, beam):
        return jnp.take_along_axis(parent_of[step_idx], beam[None, :], axis=0)[0]

    def cache_at(step_idx):
        ancestor = own_beam
        new_parts = [None] * (step_idx + 1)
        new_parts[step_idx] = fresh[:, step_idx]
        for back in range(step_idx, 0, -1):
            ancestor = climb(back, ancestor)
            new_parts[back - 1] = pick_rows(
                [f[:, back - 1] for f in fresh_all], hop_of(ancestor), 1
            )
        ancestor = climb(0, ancestor)
        past_part = pick_rows(past_all, hop_of(ancestor), 1)
        return jnp.concatenate([past_part] + [n[:, :, None, :] for n in new_parts], axis=2)

    contexts = []
    final_cache = None
    for step_idx in range(steps):
        cache = cache_at(step_idx)
        if step_idx == steps - 1:
            final_cache = cache
        query = new_query[step_idx]
        scores = (
            jnp.einsum("rd,rpd->rp", query, cache[0], preferred_element_type=jnp.float32)
            * scaling
        )
        highest = jnp.max(scores, axis=1, keepdims=True)
        raw_weights = jnp.exp(scores - highest)
        totals = jnp.sum(raw_weights, axis=1, keepdims=True)
        summed = jnp.einsum(
            "rp,rpd->rd",
            raw_weights,
            cache[1].astype(jnp.float32),
            preferred_element_type=jnp.float32,
        )
        contexts.append((summed / totals).astype(jnp.bfloat16))
    self_context = jnp.stack(contexts).reshape(steps * row_count, head_width)
    partial_out = jnp.dot(self_context, self_wo, preferred_element_type=jnp.float32)
    summed_out = ring_sum(partial_out.astype(jnp.bfloat16), "head")
    residual = hidden_in + summed_out.reshape(hidden_in.shape)
    normed_cross = rms_scaled(residual, cross_gain).astype(jnp.bfloat16)
    cross_query = jnp.dot(
        normed_cross.reshape(steps * row_count, -1), cross_wq, preferred_element_type=jnp.float32
    ).astype(jnp.bfloat16)
    by_doc = cross_query.reshape(steps, docs_here, TARGETS, head_width)

    sent = []
    for shift in range(BEAMS):
        route = [
            (beam * group_size + slot, slot * docs_here + (beam + shift) % BEAMS)
            for beam in range(BEAMS)
            for slot in range(group_size)
        ]
        piece = lax.dynamic_index_in_dim(by_doc, (my_beam + shift) % BEAMS, 1, keepdims=False)
        sent.append(lax.ppermute(piece, "hyp", route))
    doc_queries = jnp.stack(sent).reshape(BEAMS * steps * TARGETS, head_width)
    answer = cross_attend(doc_queries, cross_keys, cross_values, doc_length, scaling)
    answer = answer.reshape(BEAMS, steps, TARGETS, head_width)

    back = []
    for shift in range(BEAMS):
        route = [
            (slot * docs_here + (beam + shift) % BEAMS, beam * group_size + slot)
            for beam in range(BEAMS)
            for slot in range(group_size)
        ]
        back.append(lax.ppermute(answer[shift], "hyp", route))
    back = jnp.stack(back)
    order = (jnp.arange(docs_here, dtype=jnp.int32) - my_beam) % BEAMS
    by_k = jnp.take(back, order, axis=0)
    contexts_out = by_k.transpose(1, 0, 2, 3).reshape(steps, row_count, head_width)
    return (contexts_out, final_cache[0], final_cache[1])


def solution(mesh):
    return jax.shard_map(
        shards,
        mesh=mesh,
        in_specs=(
            P(None, "hyp", None),
            P(),
            P(),
            P(),
            P(None, "head"),
            P(None, "head"),
            P(None, "head"),
            P("head", None),
            P(),
            P(None, "head"),
            P("hyp", "head"),
            P("hyp", "head"),
            P("hyp"),
            P("hyp", None, "head"),
            P("hyp", None, "head"),
            P(),
        ),
        out_specs=(P(None, "hyp", "head"), P("hyp", None, "head"), P("hyp", None, "head")),
        check_vma=False,
    )
```

```python
import jax
import jax.numpy as jnp
from jax import lax
from jax.sharding import PartitionSpec as P


HEAD = 256
BEAMS = 4
TARGETS = 4


EPSILON = 1e-06


def rms_scaled(values_in, gain):
    mean_square = jnp.mean(values_in * values_in, axis=-1, keepdims=True)
    return values_in * lax.rsqrt(mean_square + EPSILON) * gain


def pick_rows(candidates, selector, row_axis):
    shape_list = [1] * candidates[0].ndim
    shape_list[row_axis] = selector.shape[0]
    chosen = candidates[0]
    for position in range(1, len(candidates)):
        chosen = jnp.where((selector == position).reshape(shape_list), candidates[position], chosen)
    return chosen


def beam_copies(block, hyp_count, group_size):
    copies = [block]
    for hop in range(1, BEAMS):
        distance = hop * group_size
        route = [((i - distance) % hyp_count, i) for i in range(hyp_count)]
        copies.append(lax.ppermute(block, "hyp", route))
    return copies


def ring_project(block, weights, axis):
    count = lax.axis_size(axis)
    me = lax.axis_index(axis)
    width = block.shape[1]
    right = [(i, (i + 1) % count) for i in range(count)]
    left = [(i, (i - 1) % count) for i in range(count)]

    def partial(piece, offset):
        source = (me + offset) % count
        w = lax.dynamic_slice_in_dim(weights, source * width, width, 0)
        return jnp.dot(piece, w, preferred_element_type=jnp.float32)

    total = partial(block, 0)
    from_left = block
    from_right = block
    for hop in range(1, count // 2):
        from_left = lax.ppermute(from_left, axis, right)
        from_right = lax.ppermute(from_right, axis, left)
        total = total + partial(from_left, -hop) + partial(from_right, hop)
    if count % 2 == 0 and count > 1:
        half = block.shape[0] // 2
        top = lax.ppermute(from_left[:half], axis, right)
        bottom = lax.ppermute(from_right[half:], axis, left)
        last = jnp.concatenate([top, bottom], axis=0)
        total = total + partial(last, count // 2)
    return total


def ring_sum(block, axis):
    count = lax.axis_size(axis)
    right = [(i, (i + 1) % count) for i in range(count)]
    left = [(i, (i - 1) % count) for i in range(count)]
    total = block.astype(jnp.float32)
    from_left = block
    from_right = block
    for _ in range(1, count // 2):
        from_left = lax.ppermute(from_left, axis, right)
        from_right = lax.ppermute(from_right, axis, left)
        total = total + from_left.astype(jnp.float32) + from_right.astype(jnp.float32)
    if count % 2 == 0 and count > 1:
        half = block.shape[0] // 2
        top = lax.ppermute(from_left[:half], axis, right)
        bottom = lax.ppermute(from_right[half:], axis, left)
        total = total + jnp.concatenate([top, bottom], axis=0).astype(jnp.float32)
    return total


def cross_attend(queries, cross_keys, cross_values, doc_length, scaling):
    scores = (
        jnp.einsum("qd,jd->qj", queries, cross_keys, preferred_element_type=jnp.float32) * scaling
    )
    live_mask = lax.broadcasted_iota(jnp.int32, (1, cross_keys.shape[0]), 1) < doc_length
    scores = jnp.where(live_mask, scores, -jnp.inf)
    highest = jnp.max(scores, axis=1, keepdims=True)
    raw_weights = jnp.exp(scores - highest)
    totals = jnp.sum(raw_weights, axis=1, keepdims=True)
    weights = (raw_weights / totals).astype(jnp.bfloat16)
    output = jnp.einsum("qj,jd->qd", weights, cross_values, preferred_element_type=jnp.float32)
    return output.astype(jnp.bfloat16)


def shards(
    step_embeds,
    lang_table,
    lang_ids,
    self_gain,
    self_wq,
    self_wk,
    self_wv,
    self_wo,
    cross_gain,
    cross_wq,
    cross_wkv,
    encoder_rows,
    doc_lengths,
    past_keys,
    past_values,
    parents,
):
    hyp_count = lax.axis_size("hyp")
    group_size = hyp_count // BEAMS
    my_index = lax.axis_index("hyp")
    my_beam = my_index // group_size
    my_slot = my_index % group_size
    steps = step_embeds.shape[0]
    row_count = step_embeds.shape[1]
    docs_here = row_count // TARGETS
    head_width = self_wq.shape[1]
    doc_count = lang_ids.shape[0]
    scaling = HEAD ** (-0.5)

    full_weights = lax.all_gather(cross_wkv, "hyp", axis=0, tiled=True)
    cross_kv = ring_project(encoder_rows, full_weights, "head").astype(jnp.bfloat16)
    cross_kv = cross_kv.reshape(encoder_rows.shape[0], 2, HEAD)
    cross_keys = cross_kv[:, 0, :]
    cross_values = cross_kv[:, 1, :]
    doc_length = doc_lengths[0]

    past_stack = jnp.stack([past_keys, past_values])
    past_all = beam_copies(past_stack, hyp_count, group_size)

    my_langs = lax.dynamic_slice_in_dim(lang_ids, my_slot * docs_here, docs_here, 0).reshape(row_count)
    one_hot = (
        my_langs[:, None] == lax.broadcasted_iota(jnp.int32, (1, lang_table.shape[0]), 1)
    ).astype(jnp.bfloat16)
    lang_rows = jnp.dot(one_hot, lang_table, preferred_element_type=jnp.float32)

    hidden_in = step_embeds.astype(jnp.float32) + lang_rows[None]
    normed = rms_scaled(hidden_in, self_gain).astype(jnp.bfloat16)
    normed = normed.reshape(steps * row_count, -1)
    new_query = jnp.dot(normed, self_wq, preferred_element_type=jnp.float32)
    new_key = jnp.dot(normed, self_wk, preferred_element_type=jnp.float32)
    new_value = jnp.dot(normed, self_wv, preferred_element_type=jnp.float32)
    new_query = new_query.astype(jnp.bfloat16)
    new_key = new_key.astype(jnp.bfloat16)
    new_value = new_value.astype(jnp.bfloat16)
    new_query = new_query.reshape(steps, row_count, head_width)
    fresh = jnp.stack([new_key, new_value]).reshape(2, steps, row_count, head_width)
    fresh_all = beam_copies(fresh, hyp_count, group_size)

    parent_view = parents.reshape(steps, BEAMS, doc_count * TARGETS)
    parent_of = lax.dynamic_slice_in_dim(parent_view, my_slot * row_count, row_count, 2)
    own_beam = jnp.full((row_count,), my_beam, jnp.int32)

    def hop_of(beam):
        return (my_beam - beam) % BEAMS

    def climb(step_idx, beam):
        return jnp.take_along_axis(parent_of[step_idx], beam[None, :], axis=0)[0]

    def cache_at(step_idx):
        ancestor = own_beam
        new_parts = [None] * (step_idx + 1)
        new_parts[step_idx] = fresh[:, step_idx]
        for back in range(step_idx, 0, -1):
            ancestor = climb(back, ancestor)
            new_parts[back - 1] = pick_rows(
                [f[:, back - 1] for f in fresh_all], hop_of(ancestor), 1
            )
        ancestor = climb(0, ancestor)
        past_part = pick_rows(past_all, hop_of(ancestor), 1)
        return jnp.concatenate([past_part] + [n[:, :, None, :] for n in new_parts], axis=2)

    contexts = []
    final_cache = None
    for step_idx in range(steps):
        cache = cache_at(step_idx)
        if step_idx == steps - 1:
            final_cache = cache
        query = new_query[step_idx]
        scores = (
            jnp.einsum("rd,rpd->rp", query, cache[0], preferred_element_type=jnp.float32)
            * scaling
        )
        highest = jnp.max(scores, axis=1, keepdims=True)
        raw_weights = jnp.exp(scores - highest)
        totals = jnp.sum(raw_weights, axis=1, keepdims=True)
        summed = jnp.einsum(
            "rp,rpd->rd",
            raw_weights,
            cache[1].astype(jnp.float32),
            preferred_element_type=jnp.float32,
        )
        contexts.append((summed / totals).astype(jnp.bfloat16))
    self_context = jnp.stack(contexts).reshape(steps * row_count, head_width)
    partial_out = jnp.dot(self_context, self_wo, preferred_element_type=jnp.float32)
    parts = partial_out.astype(jnp.bfloat16)
    split = (steps - 1) * row_count
    every_part = lax.all_gather(parts[:split], "head", axis=0, tiled=False)
    early_sum = jnp.sum(every_part.astype(jnp.float32), axis=0)
    late_sum = ring_sum(parts[split:], "head")
    summed_out = jnp.concatenate([early_sum, late_sum], axis=0)
    residual = hidden_in + summed_out.reshape(hidden_in.shape)
    normed_cross = rms_scaled(residual, cross_gain).astype(jnp.bfloat16)
    cross_query = jnp.dot(
        normed_cross.reshape(steps * row_count, -1), cross_wq, preferred_element_type=jnp.float32
    ).astype(jnp.bfloat16)
    by_doc = cross_query.reshape(steps, docs_here, TARGETS, head_width)

    sent = []
    for shift in range(BEAMS):
        route = [
            (beam * group_size + slot, slot * docs_here + (beam + shift) % BEAMS)
            for beam in range(BEAMS)
            for slot in range(group_size)
        ]
        piece = lax.dynamic_index_in_dim(by_doc, (my_beam + shift) % BEAMS, 1, keepdims=False)
        sent.append(lax.ppermute(piece, "hyp", route))
    doc_queries = jnp.stack(sent).reshape(BEAMS * steps * TARGETS, head_width)
    answer = cross_attend(doc_queries, cross_keys, cross_values, doc_length, scaling)
    answer = answer.reshape(BEAMS, steps, TARGETS, head_width)

    back = []
    for shift in range(BEAMS):
        route = [
            (slot * docs_here + (beam + shift) % BEAMS, beam * group_size + slot)
            for beam in range(BEAMS)
            for slot in range(group_size)
        ]
        back.append(lax.ppermute(answer[shift], "hyp", route))
    back = jnp.stack(back)
    order = (jnp.arange(docs_here, dtype=jnp.int32) - my_beam) % BEAMS
    by_k = jnp.take(back, order, axis=0)
    contexts_out = by_k.transpose(1, 0, 2, 3).reshape(steps, row_count, head_width)
    return (contexts_out, final_cache[0], final_cache[1])


def solution(mesh):
    return jax.shard_map(
        shards,
        mesh=mesh,
        in_specs=(
            P(None, "hyp", None),
            P(),
            P(),
            P(),
            P(None, "head"),
            P(None, "head"),
            P(None, "head"),
            P("head", None),
            P(),
            P(None, "head"),
            P("hyp", "head"),
            P("hyp", "head"),
            P("hyp"),
            P("hyp", None, "head"),
            P("hyp", None, "head"),
            P(),
        ),
        out_specs=(P(None, "hyp", "head"), P("hyp", None, "head"), P("hyp", None, "head")),
        check_vma=False,
    )
```

```python
import jax
import jax.numpy as jnp
from jax import lax
from jax.sharding import PartitionSpec as P


HEAD = 256
BEAMS = 4
TARGETS = 4


EPSILON = 1e-06


def rms_scaled(values_in, gain):
    mean_square = jnp.mean(values_in * values_in, axis=-1, keepdims=True)
    return values_in * lax.rsqrt(mean_square + EPSILON) * gain


def pick_rows(candidates, selector, row_axis):
    shape_list = [1] * candidates[0].ndim
    shape_list[row_axis] = selector.shape[0]
    chosen = candidates[0]
    for position in range(1, len(candidates)):
        chosen = jnp.where((selector == position).reshape(shape_list), candidates[position], chosen)
    return chosen


def beam_copies(block, hyp_count, group_size):
    copies = [block]
    for hop in range(1, BEAMS):
        distance = hop * group_size
        route = [((i - distance) % hyp_count, i) for i in range(hyp_count)]
        copies.append(lax.ppermute(block, "hyp", route))
    return copies


def ring_project(block, weights, axis):
    count = lax.axis_size(axis)
    me = lax.axis_index(axis)
    width = block.shape[1]
    right = [(i, (i + 1) % count) for i in range(count)]
    left = [(i, (i - 1) % count) for i in range(count)]

    def partial(piece, offset):
        source = (me + offset) % count
        w = lax.dynamic_slice_in_dim(weights, source * width, width, 0)
        return jnp.dot(piece, w, preferred_element_type=jnp.float32)

    total = partial(block, 0)
    from_left = block
    from_right = block
    for hop in range(1, count // 2):
        from_left = lax.ppermute(from_left, axis, right)
        from_right = lax.ppermute(from_right, axis, left)
        total = total + partial(from_left, -hop) + partial(from_right, hop)
    if count % 2 == 0 and count > 1:
        half = block.shape[0] // 2
        top = lax.ppermute(from_left[:half], axis, right)
        bottom = lax.ppermute(from_right[half:], axis, left)
        last = jnp.concatenate([top, bottom], axis=0)
        total = total + partial(last, count // 2)
    return total


def cross_attend(queries, cross_keys, cross_values, doc_length, scaling):
    scores = (
        jnp.einsum("qd,jd->qj", queries, cross_keys, preferred_element_type=jnp.float32) * scaling
    )
    live_mask = lax.broadcasted_iota(jnp.int32, (1, cross_keys.shape[0]), 1) < doc_length
    scores = jnp.where(live_mask, scores, -jnp.inf)
    highest = jnp.max(scores, axis=1, keepdims=True)
    raw_weights = jnp.exp(scores - highest)
    totals = jnp.sum(raw_weights, axis=1, keepdims=True)
    weights = (raw_weights / totals).astype(jnp.bfloat16)
    output = jnp.einsum("qj,jd->qd", weights, cross_values, preferred_element_type=jnp.float32)
    return output.astype(jnp.bfloat16)


def shards(
    step_embeds,
    lang_table,
    lang_ids,
    self_gain,
    self_wq,
    self_wk,
    self_wv,
    self_wo,
    cross_gain,
    cross_wq,
    cross_wkv,
    encoder_rows,
    doc_lengths,
    past_keys,
    past_values,
    parents,
):
    hyp_count = lax.axis_size("hyp")
    group_size = hyp_count // BEAMS
    my_index = lax.axis_index("hyp")
    my_beam = my_index // group_size
    my_slot = my_index % group_size
    steps = step_embeds.shape[0]
    row_count = step_embeds.shape[1]
    docs_here = row_count // TARGETS
    head_width = self_wq.shape[1]
    doc_count = lang_ids.shape[0]
    scaling = HEAD ** (-0.5)

    full_weights = lax.all_gather(cross_wkv, "hyp", axis=0, tiled=True)
    cross_kv = ring_project(encoder_rows, full_weights, "head").astype(jnp.bfloat16)
    cross_kv = cross_kv.reshape(encoder_rows.shape[0], 2, HEAD)
    cross_keys = cross_kv[:, 0, :]
    cross_values = cross_kv[:, 1, :]
    doc_length = doc_lengths[0]

    past_stack = jnp.stack([past_keys, past_values])
    past_all = beam_copies(past_stack, hyp_count, group_size)

    my_langs = lax.dynamic_slice_in_dim(lang_ids, my_slot * docs_here, docs_here, 0).reshape(row_count)
    one_hot = (
        my_langs[:, None] == lax.broadcasted_iota(jnp.int32, (1, lang_table.shape[0]), 1)
    ).astype(jnp.bfloat16)
    lang_rows = jnp.dot(one_hot, lang_table, preferred_element_type=jnp.float32)

    hidden_in = step_embeds.astype(jnp.float32) + lang_rows[None]
    normed = rms_scaled(hidden_in, self_gain).astype(jnp.bfloat16)
    normed = normed.reshape(steps * row_count, -1)
    new_query = jnp.dot(normed, self_wq, preferred_element_type=jnp.float32)
    new_key = jnp.dot(normed, self_wk, preferred_element_type=jnp.float32)
    new_value = jnp.dot(normed, self_wv, preferred_element_type=jnp.float32)
    new_query = new_query.astype(jnp.bfloat16)
    new_key = new_key.astype(jnp.bfloat16)
    new_value = new_value.astype(jnp.bfloat16)
    new_query = new_query.reshape(steps, row_count, head_width)
    fresh = jnp.stack([new_key, new_value]).reshape(2, steps, row_count, head_width)
    fresh_all = beam_copies(fresh, hyp_count, group_size)

    parent_view = parents.reshape(steps, BEAMS, doc_count * TARGETS)
    parent_of = lax.dynamic_slice_in_dim(parent_view, my_slot * row_count, row_count, 2)
    own_beam = jnp.full((row_count,), my_beam, jnp.int32)

    def hop_of(beam):
        return (my_beam - beam) % BEAMS

    def climb(step_idx, beam):
        return jnp.take_along_axis(parent_of[step_idx], beam[None, :], axis=0)[0]

    def cache_at(step_idx):
        ancestor = own_beam
        new_parts = [None] * (step_idx + 1)
        new_parts[step_idx] = fresh[:, step_idx]
        for back in range(step_idx, 0, -1):
            ancestor = climb(back, ancestor)
            new_parts[back - 1] = pick_rows(
                [f[:, back - 1] for f in fresh_all], hop_of(ancestor), 1
            )
        ancestor = climb(0, ancestor)
        past_part = pick_rows(past_all, hop_of(ancestor), 1)
        return jnp.concatenate([past_part] + [n[:, :, None, :] for n in new_parts], axis=2)

    contexts = []
    final_cache = None
    for step_idx in range(steps):
        cache = cache_at(step_idx)
        if step_idx == steps - 1:
            final_cache = cache
        query = new_query[step_idx]
        scores = (
            jnp.einsum("rd,rpd->rp", query, cache[0], preferred_element_type=jnp.float32)
            * scaling
        )
        highest = jnp.max(scores, axis=1, keepdims=True)
        raw_weights = jnp.exp(scores - highest)
        totals = jnp.sum(raw_weights, axis=1, keepdims=True)
        summed = jnp.einsum(
            "rp,rpd->rd",
            raw_weights,
            cache[1].astype(jnp.float32),
            preferred_element_type=jnp.float32,
        )
        contexts.append((summed / totals).astype(jnp.bfloat16))
    self_context = jnp.stack(contexts).reshape(steps * row_count, head_width)
    partial_out = jnp.dot(self_context, self_wo, preferred_element_type=jnp.float32)
    every_part = lax.all_gather(partial_out.astype(jnp.bfloat16), "head", axis=0, tiled=False)
    summed_out = jnp.sum(every_part.astype(jnp.float32), axis=0)
    residual = hidden_in + summed_out.reshape(hidden_in.shape)
    normed_cross = rms_scaled(residual, cross_gain).astype(jnp.bfloat16)
    cross_query = jnp.dot(
        normed_cross.reshape(steps * row_count, -1), cross_wq, preferred_element_type=jnp.float32
    ).astype(jnp.bfloat16)
    by_doc = cross_query.reshape(steps, docs_here, TARGETS, head_width)

    sent = []
    for shift in range(BEAMS):
        route = [
            (beam * group_size + slot, slot * docs_here + (beam + shift) % BEAMS)
            for beam in range(BEAMS)
            for slot in range(group_size)
        ]
        piece = lax.dynamic_index_in_dim(by_doc, (my_beam + shift) % BEAMS, 1, keepdims=False)
        sent.append(lax.ppermute(piece, "hyp", route))
    back = []
    for shift in range(BEAMS):
        message = sent[shift].reshape(steps * TARGETS, head_width)
        answer = cross_attend(message, cross_keys, cross_values, doc_length, scaling)
        route = [
            (slot * docs_here + (beam + shift) % BEAMS, beam * group_size + slot)
            for beam in range(BEAMS)
            for slot in range(group_size)
        ]
        back.append(lax.ppermute(answer.reshape(steps, TARGETS, head_width), "hyp", route))
    back = jnp.stack(back)
    order = (jnp.arange(docs_here, dtype=jnp.int32) - my_beam) % BEAMS
    by_k = jnp.take(back, order, axis=0)
    contexts_out = by_k.transpose(1, 0, 2, 3).reshape(steps, row_count, head_width)
    return (contexts_out, final_cache[0], final_cache[1])


def solution(mesh):
    return jax.shard_map(
        shards,
        mesh=mesh,
        in_specs=(
            P(None, "hyp", None),
            P(),
            P(),
            P(),
            P(None, "head"),
            P(None, "head"),
            P(None, "head"),
            P("head", None),
            P(),
            P(None, "head"),
            P("hyp", "head"),
            P("hyp", "head"),
            P("hyp"),
            P("hyp", None, "head"),
            P("hyp", None, "head"),
            P(),
        ),
        out_specs=(P(None, "hyp", "head"), P("hyp", None, "head"), P("hyp", None, "head")),
        check_vma=False,
    )
```
